512 devices in a mesh: dp: 16 (over y, z_lo), page: 32 (over z_hi, x, core).
Axes of the slice: x: 4, y: 4, z: 16 (z_hi: 4, z_lo: 4; z = z_hi * 4 + z_lo), core: 2. Of those that a mesh axis runs over, the one named last changes fastest.
Arguments:
- queries: bfloat16 [16, 32, 128, 1024], P('dp', 'page'), may hold values from -200 to 200
- keys: bfloat16 [16, 32, 128, 1024], P('dp', 'page'), may hold values from -6 to 6
- values: bfloat16 [16, 32, 128, 1024], P('dp', 'page'), may hold values from -6 to 6
- grad_out: bfloat16 [16, 32, 128, 1024], P('dp', 'page'), may hold values from -6 to 6
- out_weight: bfloat16 [1024, 1024], P(('dp', 'page')), may hold values from -0.1875 to 0.1875
- partners: int32 [16, 2, 32], P('dp'), may hold values from 0 to 31, as said below
- block_mask: int32 [16, 32, 2, 1, 1], P('dp', 'page'), may hold values 0 or 1
- buckets: int32 [16, 32, 3, 1, 1], P('dp', 'page'), may hold values from 0 to 31
- bias_table: float32 [32, 16], replicated, may hold values from -4 to 4
Outputs:
- layer_out: bfloat16 [16, 32, 128, 1024], P('dp', 'page')
- query_grad: bfloat16 [16, 32, 128, 1024], P('dp', 'page')
- key_grad: bfloat16 [16, 32, 128, 1024], P('dp', 'page')
- value_grad: bfloat16 [16, 32, 128, 1024], P('dp', 'page')
- weight_grad: float32 [1024, 1024], P(('dp', 'page'))
The draws below stay inside these ranges and needn't reach their ends.
Inputs may be any that keep to these rules, and one draw needn't show every extreme that they name: partners[f, r, partners[f, r, p]] = p and partners[f, r, p] != p.
All inputs are finite; a program needn't handle non-finite values. No bound on the sum of `block_mask` on one device may be relied on, other than what follows from the above.
Results may differ from the reference program's by a relative error of at most 0.025.
Values may be sent and summed in bfloat16 or wider, within the bound.
No kernel may reach another device: no remote copies, remote signals or barrier semaphores. Data moves between devices by JAX's collectives and lax.ppermute only.
A program may use at most 64 MiB of HBM per device.

```python
import math
import jax
import jax.numpy as jnp
from jax import lax

D = 1024
H = 16
PAGE = 128
BLOCK = 128
NB = 1
ROUNDS = 2
NBUCKET = 32
FILINGS = 16
PAGES = 32


def paired_draw(key):
    shape = (FILINGS, PAGES, PAGE, D)
    key_vals = jax.random.truncated_normal(jax.random.fold_in(key, 11), -6.0, 6.0, shape, jnp.float32)
    query_vals = jax.random.truncated_normal(jax.random.fold_in(key, 12), -6.0, 6.0, shape, jnp.float32)
    return (query_vals, key_vals)


def draw_queries(key, part):
    return paired_draw(key)[0].astype(jnp.bfloat16)


def draw_keys(key, part):
    return paired_draw(key)[1].astype(jnp.bfloat16)


def draw_partners(key, part):
    sub_keys = jax.random.split(key, FILINGS * ROUNDS)

    def one_matching(sub_key):
        order = jax.random.permutation(sub_key, PAGES).astype(jnp.int32)
        mate_of = order[jnp.arange(PAGES, dtype=jnp.int32) ^ 1]
        return jnp.zeros((PAGES,), jnp.int32).at[order].set(mate_of)
    return jax.vmap(one_matching)(sub_keys).reshape(FILINGS, ROUNDS, PAGES)


def with_ends(values, stream_key, smallest, largest):
    longest = values.shape.index(max(values.shape))
    spots = []
    for shift in (0, 1):
        where = [jax.random.randint(jax.random.fold_in(stream_key, axis), (), 0, length) for axis, length in enumerate(values.shape)]
        where[longest] = (where[longest] + shift) % values.shape[longest]
        spots.append(tuple(where))
    return values.at[spots[0]].set(smallest).at[spots[1]].set(largest)


def steps_of(rng, dims, cuts, smallest, top_value):
    level, own = 1.0, jax.random.fold_in(rng, 6)
    for dim, shards_of in cuts:
        heights = jnp.exp(jax.random.uniform(jax.random.fold_in(own, dim), (shards_of,), jnp.float32, smallest / len(cuts), top_value / len(cuts)))
        level = level * jnp.repeat(heights, dims[dim] // shards_of).reshape([-1 if axis == dim else 1 for axis in range(len(dims))])
    return level


def normal_values(stream_key, shape, scale, limit, cuts=(), kind=jnp.bfloat16):
    level = steps_of(stream_key, shape, cuts, -0.22, 0.18) if cuts else 1.0
    values = jax.random.normal(stream_key, shape, jnp.float32) * scale * level
    return jnp.minimum(jnp.maximum(values, -limit), limit).astype(kind)


def setup_inputs(seed: int = 0) -> dict:
    splits = jax.random.split(jax.random.key(seed), 10)
    return {
        "queries": draw_queries(jax.random.fold_in(splits[9], 71), 0),
        "keys": draw_keys(jax.random.fold_in(splits[9], 71), 0),
        "values": normal_values(splits[2], (FILINGS, PAGES, PAGE, D), 1.0, 6.0, ((0, 16), (1, 32))),
        "grad_out": normal_values(splits[3], (FILINGS, PAGES, PAGE, D), 1.0, 6.0, ((0, 16), (1, 32))),
        "out_weight": normal_values(splits[4], (D, D), D ** -0.5, 0.1875, ((0, 512),)),
        "partners": draw_partners(jax.random.fold_in(splits[9], 71), 0),
        "block_mask": with_ends((jax.random.randint(splits[6], (FILINGS, PAGES, ROUNDS, NB, NB), 0, 2) < 1).astype(jnp.int32), jax.random.fold_in(splits[6], 1), 0, 1),
        "buckets": with_ends(jax.random.randint(splits[7], (FILINGS, PAGES, ROUNDS + 1, NB, NB), 0, NBUCKET), jax.random.fold_in(splits[7], 1), 0, NBUCKET - 1).astype(jnp.int32),
        "bias_table": normal_values(splits[8], (NBUCKET, H), 1.0, 4.0, (), jnp.float32),
    }


heads_per_step = 4
neg_large = -1e+30

def head_steps(query_rows, key_set, value_set, grad_rows, bias_blocks, allowed):
    page_len, width = query_rows.shape
    key_count = key_set.shape[0]
    groups = key_count // page_len
    head_dim = width // H
    step_count = H // heads_per_step
    block_count = page_len // BLOCK
    scale = 1.0 / math.sqrt(head_dim)

    def split(array):
        return array.reshape(array.shape[0], step_count, heads_per_step, head_dim).transpose(1, 0, 2, 3)
    bias_split = bias_blocks.reshape(groups, block_count, block_count, step_count, heads_per_step).transpose(3, 4, 1, 0, 2)
    allow_wide = allowed.transpose(1, 0, 2)[None, :, None, :, :, None]

    def one_step(inputs):
        q_part, k_part, v_part, g_part, b_part = inputs
        q_wide = q_part.astype(jnp.float32)
        k_wide = k_part.astype(jnp.float32)
        v_wide = v_part.astype(jnp.float32)
        g_wide = g_part.astype(jnp.float32)
        scores = jnp.einsum('qhd,khd->hqk', q_wide, k_wide) * scale
        scores = scores.reshape(heads_per_step, block_count, BLOCK, groups, block_count, BLOCK)
        scores = scores + b_part[:, :, None, :, :, None]
        scores = jnp.where(allow_wide, scores, neg_large).reshape(heads_per_step, page_len, key_count)
        top = lax.optimization_barrier(jnp.max(scores, axis=-1, keepdims=True))
        expo = jnp.exp(scores - top)
        prob = expo / lax.optimization_barrier(jnp.sum(expo, axis=-1, keepdims=True))
        prob_b = prob.astype(jnp.bfloat16)
        attn_part = jnp.einsum('hqk,khd->qhd', prob_b.astype(jnp.float32), v_wide).astype(jnp.bfloat16)
        dprob = jnp.einsum('qhd,khd->hqk', g_wide, v_wide)
        row_dot = lax.optimization_barrier(jnp.sum(g_wide * attn_part.astype(jnp.float32), axis=-1)).T[:, :, None]
        dscore = (prob * (dprob - row_dot) * scale).astype(jnp.bfloat16)
        ds_wide = dscore.astype(jnp.float32)
        q_grad = jnp.einsum('hqk,khd->qhd', ds_wide, k_wide)
        k_grad = jnp.einsum('hqk,qhd->khd', ds_wide, q_wide)
        v_grad = jnp.einsum('hqk,qhd->khd', prob_b.astype(jnp.float32), g_wide)
        return (attn_part, q_grad, k_grad, v_grad)
    results = lax.map(one_step, (split(query_rows), split(key_set), split(value_set), split(grad_rows), bias_split))

    def join(array):
        return array.transpose(1, 0, 2, 3).reshape(array.shape[1], width)
    return (join(results[0]), join(results[1]), join(results[2]), join(results[3]))

def reference(queries, keys, values, grad_out, out_weight, partners, block_mask, buckets, bias_table):
    page_len = queries.shape[2]
    width = queries.shape[3]
    block_count = page_len // BLOCK

    def page_terms(weight_acc, page_index):
        filing = page_index // PAGES
        page_no = page_index % PAGES
        mates = [partners[filing, r, page_no] for r in range(ROUNDS)]
        key_set = jnp.concatenate([keys[filing, page_no]] + [keys[filing, mates[r]] for r in range(ROUNDS)], 0)
        value_set = jnp.concatenate([values[filing, page_no]] + [values[filing, mates[r]] for r in range(ROUNDS)], 0)
        grad_page = grad_out[filing, page_no]
        d_attn = jnp.dot(grad_page, out_weight.T, preferred_element_type=jnp.float32).astype(jnp.bfloat16)
        bias_blocks = bias_table[buckets[filing, page_no]]
        allowed = jnp.concatenate([jnp.ones((1, block_count, block_count), bool), block_mask[filing, page_no] == 1], 0)
        attn, q_grad, k_grad, v_grad = head_steps(queries[filing, page_no], key_set, value_set, d_attn, bias_blocks, allowed)
        layer_page = jnp.dot(attn, out_weight, preferred_element_type=jnp.float32).astype(jnp.bfloat16)
        weight_acc = weight_acc + jnp.dot(attn.T, grad_page, preferred_element_type=jnp.float32)
        own_k = k_grad[:page_len]
        own_v = v_grad[:page_len]
        part_k = k_grad[page_len:].reshape(ROUNDS, page_len, width).astype(jnp.bfloat16)
        part_v = v_grad[page_len:].reshape(ROUNDS, page_len, width).astype(jnp.bfloat16)
        return (weight_acc, (layer_page, q_grad.astype(jnp.bfloat16), own_k, own_v, part_k, part_v))
    start_acc = jnp.zeros((width, width), jnp.float32)
    weight_grad, pieces = lax.scan(page_terms, start_acc, jnp.arange(FILINGS * PAGES, dtype=jnp.int32))

    def shaped(array):
        return array.reshape((FILINGS, PAGES) + array.shape[1:])
    layer_out = shaped(pieces[0])
    query_grad = shaped(pieces[1])
    own_k = shaped(pieces[2])
    own_v = shaped(pieces[3])
    part_k = shaped(pieces[4])
    part_v = shaped(pieces[5])
    total_k = own_k
    total_v = own_v
    for r in range(ROUNDS):
        mate_idx = partners[:, r, :][:, :, None, None]
        total_k = total_k + jnp.take_along_axis(part_k[:, :, r], mate_idx, axis=1).astype(jnp.float32)
        total_v = total_v + jnp.take_along_axis(part_v[:, :, r], mate_idx, axis=1).astype(jnp.float32)
    return (layer_out, query_grad, total_k.astype(jnp.bfloat16), total_v.astype(jnp.bfloat16), weight_grad)
```

```python
import math

import jax
import jax.numpy as jnp
from jax import lax
from jax.sharding import PartitionSpec as P

H = 16
BLOCK = 128
ROUNDS = 2


heads_per_step = 4
neg_large = -1e30


def head_steps(query_rows, key_set, value_set, grad_rows, bias_blocks, allowed):
    page_len, width = query_rows.shape
    key_count = key_set.shape[0]
    groups = key_count // page_len
    head_dim = width // H
    step_count = H // heads_per_step
    block_count = page_len // BLOCK
    scale = 1.0 / math.sqrt(head_dim)

    def split(array):
        return array.reshape(array.shape[0], step_count, heads_per_step, head_dim).transpose(
            1, 0, 2, 3
        )

    bias_split = bias_blocks.reshape(
        groups, block_count, block_count, step_count, heads_per_step
    ).transpose(3, 4, 1, 0, 2)
    allow_wide = allowed.transpose(1, 0, 2)[None, :, None, :, :, None]

    def one_step(inputs):
        q_part, k_part, v_part, g_part, b_part = inputs
        scores = (
            jnp.einsum("qhd,khd->hqk", q_part, k_part, preferred_element_type=jnp.float32) * scale
        )
        scores = scores.reshape(heads_per_step, block_count, BLOCK, groups, block_count, BLOCK)
        scores = scores + b_part[:, :, None, :, :, None]
        scores = jnp.where(allow_wide, scores, neg_large).reshape(
            heads_per_step, page_len, key_count
        )
        top = jnp.max(scores, axis=-1, keepdims=True)
        expo = jnp.exp(scores - top)
        prob = expo / jnp.sum(expo, axis=-1, keepdims=True)
        prob_b = prob.astype(jnp.bfloat16)
        attn_part = jnp.einsum(
            "hqk,khd->qhd", prob_b, v_part, preferred_element_type=jnp.float32
        ).astype(jnp.bfloat16)
        dprob = jnp.einsum("qhd,khd->hqk", g_part, v_part, preferred_element_type=jnp.float32)
        row_dot = jnp.sum(g_part.astype(jnp.float32) * attn_part.astype(jnp.float32), axis=-1).T[
            :, :, None
        ]
        dscore = (prob * (dprob - row_dot) * scale).astype(jnp.bfloat16)
        q_grad = jnp.einsum("hqk,khd->qhd", dscore, k_part, preferred_element_type=jnp.float32)
        k_grad = jnp.einsum("hqk,qhd->khd", dscore, q_part, preferred_element_type=jnp.float32)
        v_grad = jnp.einsum("hqk,qhd->khd", prob_b, g_part, preferred_element_type=jnp.float32)
        return (attn_part, q_grad, k_grad, v_grad)

    results = lax.map(
        one_step,
        (split(query_rows), split(key_set), split(value_set), split(grad_rows), bias_split),
    )

    def join(array):
        return array.transpose(1, 0, 2, 3).reshape(array.shape[1], width)

    return (join(results[0]), join(results[1]), join(results[2]), join(results[3]))


def shards(queries, keys, values, grad_out, out_weight, partners, block_mask, buckets, bias_table):
    weight = lax.all_gather(
        lax.all_gather(out_weight, "page", axis=0, tiled=True), "dp", axis=0, tiled=True
    )
    q_page = queries[0, 0]
    k_page = keys[0, 0]
    v_page = values[0, 0]
    g_page = grad_out[0, 0]
    page_len, width = q_page.shape
    block_count = page_len // BLOCK
    peers = lax.axis_size("page")
    piece_rows = page_len // peers
    mates = partners[0]
    kv_pair = jnp.stack([k_page, v_page])
    d_attn = lax.dot_general(
        g_page, weight, (((1,), (1,)), ((), ())), preferred_element_type=jnp.float32
    ).astype(jnp.bfloat16)

    def spread(stacked):
        pieces = stacked.reshape(2, peers, piece_rows, width)
        return lax.all_to_all(pieces, "page", split_axis=1, concat_axis=1, tiled=True)

    def collect(received, chosen):
        picked = jnp.take(received, chosen, axis=1)
        back = lax.all_to_all(picked, "page", split_axis=2, concat_axis=2, tiled=True)
        return back.reshape(2, chosen.shape[0], page_len, width)

    fetched = collect(spread(kv_pair), mates)
    key_set = jnp.concatenate([k_page[None], fetched[0]], 0).reshape(-1, width)
    value_set = jnp.concatenate([v_page[None], fetched[1]], 0).reshape(-1, width)
    bucket_ids = buckets[0, 0]
    one_hot = bucket_ids[..., None] == jnp.arange(bias_table.shape[0], dtype=jnp.int32)
    bias_blocks = jnp.sum(jnp.where(one_hot[..., None], bias_table, 0.0), axis=-2)
    allowed = jnp.concatenate(
        [jnp.ones((1, block_count, block_count), bool), block_mask[0, 0] == 1], 0
    )
    attn, q_grad, k_grad, v_grad = head_steps(
        q_page, key_set, value_set, d_attn, bias_blocks, allowed
    )
    layer_out = jnp.dot(attn, weight, preferred_element_type=jnp.float32).astype(jnp.bfloat16)
    partial = lax.dot_general(
        attn, g_page, (((0,), (0,)), ((), ())), preferred_element_type=jnp.float32
    )
    dp_size = lax.axis_size("dp")
    rows_each = width // (dp_size * peers)
    partial = partial.reshape(dp_size, peers, rows_each, width)
    partial = lax.psum_scatter(partial, "dp", scatter_dimension=0, tiled=True)
    partial = partial.reshape(1, peers, rows_each * width // 128, 128)
    partial = lax.psum_scatter(partial, "page", scatter_dimension=1, tiled=True)
    weight_grad = partial.reshape(rows_each, width)
    outgoing = (
        jnp.stack([k_grad[page_len:], v_grad[page_len:]])
        .reshape(2, ROUNDS, page_len, width)
        .astype(jnp.bfloat16)
    )

    def give_back(terms, chosen):
        round_count = terms.shape[1]
        pieces = terms.reshape(2, round_count, peers, piece_rows, width)
        received = lax.all_to_all(pieces, "page", split_axis=2, concat_axis=2, tiled=True)
        picked = jnp.stack(
            [jnp.take(received[:, r], chosen[r], axis=1) for r in range(round_count)], 1
        )
        back = lax.all_to_all(picked, "page", split_axis=2, concat_axis=2, tiled=True)
        return back.reshape(2, round_count, page_len, width)

    returned = give_back(outgoing, mates)
    totals = jnp.stack([k_grad[:page_len], v_grad[:page_len]]) + jnp.sum(
        returned.astype(jnp.float32), axis=1
    )
    key_grad = totals[0].astype(jnp.bfloat16)[None, None]
    value_grad = totals[1].astype(jnp.bfloat16)[None, None]
    return (
        layer_out[None, None],
        q_grad.astype(jnp.bfloat16)[None, None],
        key_grad,
        value_grad,
        weight_grad,
    )


def solution(mesh):
    in_specs = (
        P("dp", "page", None, None),
        P("dp", "page", None, None),
        P("dp", "page", None, None),
        P("dp", "page", None, None),
        P(("dp", "page"), None),
        P("dp", None, None),
        P("dp", "page", None, None, None),
        P("dp", "page", None, None, None),
        P(),
    )
    out_specs = (
        P("dp", "page", None, None),
        P("dp", "page", None, None),
        P("dp", "page", None, None),
        P("dp", "page", None, None),
        P(("dp", "page"), None),
    )
    return jax.shard_map(shards, mesh=mesh, in_specs=in_specs, out_specs=out_specs, check_vma=False)
```

```python
import math

import jax
import jax.numpy as jnp
from jax import lax
from jax.sharding import PartitionSpec as P

H = 16
BLOCK = 128
ROUNDS = 2


neg_large = -1e30


def attend_forward(query_rows, key_set, value_set, bias_blocks, allowed):
    page_len, width = query_rows.shape
    key_count = key_set.shape[0]
    groups = key_count // page_len
    head_dim = width // H
    block_count = page_len // BLOCK
    scale = 1.0 / math.sqrt(head_dim)
    q = query_rows.reshape(page_len, H, head_dim)
    k = key_set.reshape(key_count, H, head_dim)
    v = value_set.reshape(key_count, H, head_dim)
    scores = jnp.einsum("qhd,khd->hqk", q, k, preferred_element_type=jnp.float32) * scale
    scores = scores.reshape(H, block_count, BLOCK, groups, block_count, BLOCK)
    bias_wide = bias_blocks.transpose(3, 1, 0, 2)[:, :, None, :, :, None]
    scores = scores + bias_wide
    allow_wide = allowed.transpose(1, 0, 2)[None, :, None, :, :, None]
    scores = jnp.where(allow_wide, scores, neg_large).reshape(H, page_len, key_count)
    top = jnp.max(scores, axis=-1, keepdims=True)
    expo = jnp.exp(scores - top)
    prob = expo / jnp.sum(expo, axis=-1, keepdims=True)
    prob_b = prob.astype(jnp.bfloat16)
    attn = jnp.einsum("hqk,khd->qhd", prob_b, v, preferred_element_type=jnp.float32).astype(
        jnp.bfloat16
    )
    return attn.reshape(page_len, width), prob, prob_b


def attend_backward(query_rows, key_set, value_set, grad_rows, attn, prob, prob_b):
    page_len, width = query_rows.shape
    key_count = key_set.shape[0]
    head_dim = width // H
    scale = 1.0 / math.sqrt(head_dim)
    q = query_rows.reshape(page_len, H, head_dim)
    k = key_set.reshape(key_count, H, head_dim)
    v = value_set.reshape(key_count, H, head_dim)
    g = grad_rows.reshape(page_len, H, head_dim)
    a = attn.reshape(page_len, H, head_dim)
    dprob = jnp.einsum("qhd,khd->hqk", g, v, preferred_element_type=jnp.float32)
    row_dot = jnp.sum(g.astype(jnp.float32) * a.astype(jnp.float32), axis=-1).T[:, :, None]
    dscore = (prob * (dprob - row_dot) * scale).astype(jnp.bfloat16)
    q_grad = jnp.einsum("hqk,khd->qhd", dscore, k, preferred_element_type=jnp.float32)
    k_grad = jnp.einsum("hqk,qhd->khd", dscore, q, preferred_element_type=jnp.float32)
    v_grad = jnp.einsum("hqk,qhd->khd", prob_b, g, preferred_element_type=jnp.float32)
    return (
        q_grad.reshape(page_len, width),
        k_grad.reshape(key_count, width),
        v_grad.reshape(key_count, width),
    )


def shards(queries, keys, values, grad_out, out_weight, partners, block_mask, buckets, bias_table):
    weight = lax.all_gather(
        lax.all_gather(out_weight, "page", axis=0, tiled=True), "dp", axis=0, tiled=True
    )
    q_page = queries[0, 0]
    k_page = keys[0, 0]
    v_page = values[0, 0]
    g_page = grad_out[0, 0]
    page_len, width = q_page.shape
    block_count = page_len // BLOCK
    peers = lax.axis_size("page")
    piece_rows = page_len // peers
    mates = partners[0]
    kv_pair = jnp.stack([k_page, v_page])
    d_attn = lax.dot_general(
        g_page, weight, (((1,), (1,)), ((), ())), preferred_element_type=jnp.float32
    ).astype(jnp.bfloat16)

    def spread(stacked):
        pieces = stacked.reshape(2, peers, piece_rows, width)
        return lax.all_to_all(pieces, "page", split_axis=1, concat_axis=1, tiled=True)

    def collect(received, chosen):
        picked = jnp.take(received, chosen, axis=1)
        back = lax.all_to_all(picked, "page", split_axis=2, concat_axis=2, tiled=True)
        return back.reshape(2, chosen.shape[0], page_len, width)

    fetched = collect(spread(kv_pair), mates)
    key_set = jnp.concatenate([k_page[None], fetched[0]], 0).reshape(-1, width)
    value_set = jnp.concatenate([v_page[None], fetched[1]], 0).reshape(-1, width)
    bucket_ids = buckets[0, 0]
    one_hot = bucket_ids[..., None] == jnp.arange(bias_table.shape[0], dtype=jnp.int32)
    bias_blocks = jnp.sum(jnp.where(one_hot[..., None], bias_table, 0.0), axis=-2)
    allowed = jnp.concatenate(
        [jnp.ones((1, block_count, block_count), bool), block_mask[0, 0] == 1], 0
    )
    attn, prob, prob_b = attend_forward(q_page, key_set, value_set, bias_blocks, allowed)
    partial = lax.dot_general(
        attn, g_page, (((0,), (0,)), ((), ())), preferred_element_type=jnp.float32
    )
    dp_size = lax.axis_size("dp")
    rows_each = width // (dp_size * peers)
    partial = partial.reshape(dp_size, peers, rows_each, width)
    partial = lax.psum_scatter(partial, "dp", scatter_dimension=0, tiled=True)
    partial = partial.reshape(1, peers, rows_each * width // 128, 128)
    partial = lax.psum_scatter(partial, "page", scatter_dimension=1, tiled=True)
    weight_grad = partial.reshape(rows_each, width)
    q_grad, k_grad, v_grad = attend_backward(
        q_page, key_set, value_set, d_attn, attn, prob, prob_b
    )
    layer_out = jnp.dot(attn, weight, preferred_element_type=jnp.float32).astype(jnp.bfloat16)
    outgoing = (
        jnp.stack([k_grad[page_len:], v_grad[page_len:]])
        .reshape(2, ROUNDS, page_len, width)
        .astype(jnp.bfloat16)
    )

    def give_back(terms, chosen):
        round_count = terms.shape[1]
        pieces = terms.reshape(2, round_count, peers, piece_rows, width)
        received = lax.all_to_all(pieces, "page", split_axis=2, concat_axis=2, tiled=True)
        picked = jnp.stack(
            [jnp.take(received[:, r], chosen[r], axis=1) for r in range(round_count)], 1
        )
        back = lax.all_to_all(picked, "page", split_axis=2, concat_axis=2, tiled=True)
        return back.reshape(2, round_count, page_len, width)

    returned = give_back(outgoing, mates)
    totals = jnp.stack([k_grad[:page_len], v_grad[:page_len]]) + jnp.sum(
        returned.astype(jnp.float32), axis=1
    )
    key_grad = totals[0].astype(jnp.bfloat16)[None, None]
    value_grad = totals[1].astype(jnp.bfloat16)[None, None]
    return (
        layer_out[None, None],
        q_grad.astype(jnp.bfloat16)[None, None],
        key_grad,
        value_grad,
        weight_grad,
    )


def solution(mesh):
    in_specs = (
        P("dp", "page", None, None),
        P("dp", "page", None, None),
        P("dp", "page", None, None),
        P("dp", "page", None, None),
        P(("dp", "page"), None),
        P("dp", None, None),
        P("dp", "page", None, None, None),
        P("dp", "page", None, None, None),
        P(),
    )
    out_specs = (
        P("dp", "page", None, None),
        P("dp", "page", None, None),
        P("dp", "page", None, None),
        P("dp", "page", None, None),
        P(("dp", "page"), None),
    )
    return jax.shard_map(shards, mesh=mesh, in_specs=in_specs, out_specs=out_specs, check_vma=False)
```

```python
import math

import jax
import jax.numpy as jnp
from jax import lax
from jax.sharding import PartitionSpec as P

H = 16
BLOCK = 128
ROUNDS = 2


neg_large = -1e30


def attend_forward(query_rows, key_set, value_set, bias_blocks, allowed):
    page_len, width = query_rows.shape
    key_count = key_set.shape[0]
    groups = key_count // page_len
    head_dim = width // H
    block_count = page_len // BLOCK
    scale = 1.0 / math.sqrt(head_dim)
    q = query_rows.reshape(page_len, H, head_dim)
    k = key_set.reshape(key_count, H, head_dim)
    v = value_set.reshape(key_count, H, head_dim)
    scores = jnp.einsum("qhd,khd->hqk", q, k, preferred_element_type=jnp.float32) * scale
    scores = scores.reshape(H, block_count, BLOCK, groups, block_count, BLOCK)
    bias_wide = bias_blocks.transpose(3, 1, 0, 2)[:, :, None, :, :, None]
    scores = scores + bias_wide
    allow_wide = allowed.transpose(1, 0, 2)[None, :, None, :, :, None]
    scores = jnp.where(allow_wide, scores, neg_large).reshape(H, page_len, key_count)
    top = jnp.max(scores, axis=-1, keepdims=True)
    expo = jnp.exp(scores - top)
    prob = expo / jnp.sum(expo, axis=-1, keepdims=True)
    prob_b = prob.astype(jnp.bfloat16)
    attn = jnp.einsum("hqk,khd->qhd", prob_b, v, preferred_element_type=jnp.float32).astype(
        jnp.bfloat16
    )
    return attn.reshape(page_len, width), prob, prob_b


def attend_backward(query_rows, key_set, value_set, grad_rows, attn, prob, prob_b):
    page_len, width = query_rows.shape
    key_count = key_set.shape[0]
    head_dim = width // H
    scale = 1.0 / math.sqrt(head_dim)
    q = query_rows.reshape(page_len, H, head_dim)
    k = key_set.reshape(key_count, H, head_dim)
    v = value_set.reshape(key_count, H, head_dim)
    g = grad_rows.reshape(page_len, H, head_dim)
    a = attn.reshape(page_len, H, head_dim)
    dprob = jnp.einsum("qhd,khd->hqk", g, v, preferred_element_type=jnp.float32)
    row_dot = jnp.sum(g.astype(jnp.float32) * a.astype(jnp.float32), axis=-1).T[:, :, None]
    dscore = (prob * (dprob - row_dot) * scale).astype(jnp.bfloat16)
    q_grad = jnp.einsum("hqk,khd->qhd", dscore, k, preferred_element_type=jnp.float32)
    k_grad = jnp.einsum("hqk,qhd->khd", dscore, q, preferred_element_type=jnp.float32)
    v_grad = jnp.einsum("hqk,qhd->khd", prob_b, g, preferred_element_type=jnp.float32)
    return (
        q_grad.reshape(page_len, width),
        k_grad.reshape(key_count, width),
        v_grad.reshape(key_count, width),
    )


def shards(queries, keys, values, grad_out, out_weight, partners, block_mask, buckets, bias_table):
    page_count = lax.axis_size("page")
    copies = jnp.broadcast_to(out_weight[None], (page_count,) + out_weight.shape)
    near = lax.all_to_all(copies, "page", split_axis=0, concat_axis=0, tiled=True)
    near = near.reshape(page_count * out_weight.shape[0], out_weight.shape[1])
    weight = lax.all_gather(near, "dp", axis=0, tiled=True)
    q_page = queries[0, 0]
    k_page = keys[0, 0]
    v_page = values[0, 0]
    g_page = grad_out[0, 0]
    page_len, width = q_page.shape
    block_count = page_len // BLOCK
    peers = lax.axis_size("page")
    piece_rows = page_len // peers
    mates = partners[0]
    kv_pair = jnp.stack([k_page, v_page])
    d_attn = lax.dot_general(
        g_page, weight, (((1,), (1,)), ((), ())), preferred_element_type=jnp.float32
    ).astype(jnp.bfloat16)

    def spread(stacked):
        pieces = stacked.reshape(2, peers, piece_rows, width)
        return lax.all_to_all(pieces, "page", split_axis=1, concat_axis=1, tiled=True)

    def collect(received, chosen):
        picked = jnp.take(received, chosen, axis=1)
        back = lax.all_to_all(picked, "page", split_axis=2, concat_axis=2, tiled=True)
        return back.reshape(2, chosen.shape[0], page_len, width)

    fetched = collect(spread(kv_pair), mates)
    key_set = jnp.concatenate([k_page[None], fetched[0]], 0).reshape(-1, width)
    value_set = jnp.concatenate([v_page[None], fetched[1]], 0).reshape(-1, width)
    bucket_ids = buckets[0, 0]
    one_hot = bucket_ids[..., None] == jnp.arange(bias_table.shape[0], dtype=jnp.int32)
    bias_blocks = jnp.sum(jnp.where(one_hot[..., None], bias_table, 0.0), axis=-2)
    allowed = jnp.concatenate(
        [jnp.ones((1, block_count, block_count), bool), block_mask[0, 0] == 1], 0
    )
    attn, prob, prob_b = attend_forward(q_page, key_set, value_set, bias_blocks, allowed)
    partial = lax.dot_general(
        attn, g_page, (((0,), (0,)), ((), ())), preferred_element_type=jnp.float32
    )
    dp_size = lax.axis_size("dp")
    rows_each = width // (dp_size * peers)
    partial = partial.reshape(dp_size, peers, rows_each, width)
    partial = lax.psum_scatter(partial, "dp", scatter_dimension=0, tiled=True)
    partial = lax.all_to_all(partial, "page", split_axis=1, concat_axis=1, tiled=True)
    weight_grad = jnp.sum(partial, axis=(0, 1))
    q_grad, k_grad, v_grad = attend_backward(
        q_page, key_set, value_set, d_attn, attn, prob, prob_b
    )
    layer_out = jnp.dot(attn, weight, preferred_element_type=jnp.float32).astype(jnp.bfloat16)
    outgoing = (
        jnp.stack([k_grad[page_len:], v_grad[page_len:]])
        .reshape(2, ROUNDS, page_len, width)
        .astype(jnp.bfloat16)
    )

    def give_back(terms, chosen):
        round_count = terms.shape[1]
        pieces = terms.reshape(2, round_count, peers, piece_rows, width)
        received = lax.all_to_all(pieces, "page", split_axis=2, concat_axis=2, tiled=True)
        picked = jnp.stack(
            [jnp.take(received[:, r], chosen[r], axis=1) for r in range(round_count)], 1
        )
        back = lax.all_to_all(picked, "page", split_axis=2, concat_axis=2, tiled=True)
        return back.reshape(2, round_count, page_len, width)

    returned = give_back(outgoing, mates)
    totals = jnp.stack([k_grad[:page_len], v_grad[:page_len]]) + jnp.sum(
        returned.astype(jnp.float32), axis=1
    )
    key_grad = totals[0].astype(jnp.bfloat16)[None, None]
    value_grad = totals[1].astype(jnp.bfloat16)[None, None]
    return (
        layer_out[None, None],
        q_grad.astype(jnp.bfloat16)[None, None],
        key_grad,
        value_grad,
        weight_grad,
    )


def solution(mesh):
    in_specs = (
        P("dp", "page", None, None),
        P("dp", "page", None, None),
        P("dp", "page", None, None),
        P("dp", "page", None, None),
        P(("dp", "page"), None),
        P("dp", None, None),
        P("dp", "page", None, None, None),
        P("dp", "page", None, None, None),
        P(),
    )
    out_specs = (
        P("dp", "page", None, None),
        P("dp", "page", None, None),
        P("dp", "page", None, None),
        P("dp", "page", None, None),
        P(("dp", "page"), None),
    )
    return jax.shard_map(shards, mesh=mesh, in_specs=in_specs, out_specs=out_specs, check_vma=False)
```

```python
import math

import jax
import jax.numpy as jnp
from jax import lax
from jax.sharding import PartitionSpec as P

H = 16
BLOCK = 128
ROUNDS = 2


neg_large = -1e30


def attend_forward(query_rows, key_set, value_set, bias_blocks, allowed):
    page_len, width = query_rows.shape
    key_count = key_set.shape[0]
    groups = key_count // page_len
    head_dim = width // H
    block_count = page_len // BLOCK
    scale = 1.0 / math.sqrt(head_dim)
    q = query_rows.reshape(page_len, H, head_dim)
    k = key_set.reshape(key_count, H, head_dim)
    v = value_set.reshape(key_count, H, head_dim)
    scores = jnp.einsum("qhd,khd->hqk", q, k, preferred_element_type=jnp.float32) * scale
    scores = scores.reshape(H, block_count, BLOCK, groups, block_count, BLOCK)
    bias_wide = bias_blocks.transpose(3, 1, 0, 2)[:, :, None, :, :, None]
    scores = scores + bias_wide
    allow_wide = allowed.transpose(1, 0, 2)[None, :, None, :, :, None]
    scores = jnp.where(allow_wide, scores, neg_large).reshape(H, page_len, key_count)
    top = jnp.max(scores, axis=-1, keepdims=True)
    expo = jnp.exp(scores - top)
    prob = expo / jnp.sum(expo, axis=-1, keepdims=True)
    prob_b = prob.astype(jnp.bfloat16)
    attn = jnp.einsum("hqk,khd->qhd", prob_b, v, preferred_element_type=jnp.float32).astype(
        jnp.bfloat16
    )
    return attn.reshape(page_len, width), prob, prob_b


def attend_backward(query_rows, key_set, value_set, grad_rows, attn, prob, prob_b):
    page_len, width = query_rows.shape
    key_count = key_set.shape[0]
    head_dim = width // H
    scale = 1.0 / math.sqrt(head_dim)
    q = query_rows.reshape(page_len, H, head_dim)
    k = key_set.reshape(key_count, H, head_dim)
    v = value_set.reshape(key_count, H, head_dim)
    g = grad_rows.reshape(page_len, H, head_dim)
    a = attn.reshape(page_len, H, head_dim)
    dprob = jnp.einsum("qhd,khd->hqk", g, v, preferred_element_type=jnp.float32)
    row_dot = jnp.sum(g.astype(jnp.float32) * a.astype(jnp.float32), axis=-1).T[:, :, None]
    dscore = (prob * (dprob - row_dot) * scale).astype(jnp.bfloat16)
    q_grad = jnp.einsum("hqk,khd->qhd", dscore, k, preferred_element_type=jnp.float32)
    k_grad = jnp.einsum("hqk,qhd->khd", dscore, q, preferred_element_type=jnp.float32)
    v_grad = jnp.einsum("hqk,qhd->khd", prob_b, g, preferred_element_type=jnp.float32)
    return (
        q_grad.reshape(page_len, width),
        k_grad.reshape(key_count, width),
        v_grad.reshape(key_count, width),
    )


def halving_scatter(blocks, axis, size):
    if size & (size - 1):
        return lax.psum_scatter(blocks, axis, scatter_dimension=0, tiled=True)
    me = lax.axis_index(axis)
    half = size // 2
    while half >= 1:
        upper = (me // half) % 2
        keep = lax.dynamic_slice_in_dim(blocks, upper * half, half, axis=0)
        send = lax.dynamic_slice_in_dim(blocks, (1 - upper) * half, half, axis=0)
        pairs = [(i, i ^ half) for i in range(size)]
        blocks = keep + lax.ppermute(send, axis, perm=pairs)
        half //= 2
    return blocks


def shards(queries, keys, values, grad_out, out_weight, partners, block_mask, buckets, bias_table):
    page_count = lax.axis_size("page")
    copies = jnp.broadcast_to(out_weight[None], (page_count,) + out_weight.shape)
    near = lax.all_to_all(copies, "page", split_axis=0, concat_axis=0, tiled=True)
    near = near.reshape(page_count * out_weight.shape[0], out_weight.shape[1])
    weight = lax.all_gather(near, "dp", axis=0, tiled=True)
    q_page = queries[0, 0]
    k_page = keys[0, 0]
    v_page = values[0, 0]
    g_page = grad_out[0, 0]
    page_len, width = q_page.shape
    block_count = page_len // BLOCK
    peers = lax.axis_size("page")
    piece_rows = page_len // peers
    mates = partners[0]
    kv_pair = jnp.stack([k_page, v_page])
    d_attn = lax.dot_general(
        g_page, weight, (((1,), (1,)), ((), ())), preferred_element_type=jnp.float32
    ).astype(jnp.bfloat16)

    def spread(stacked):
        pieces = stacked.reshape(2, peers, piece_rows, width)
        return lax.all_to_all(pieces, "page", split_axis=1, concat_axis=1, tiled=True)

    def collect(received, chosen):
        picked = jnp.take(received, chosen, axis=1)
        back = lax.all_to_all(picked, "page", split_axis=2, concat_axis=2, tiled=True)
        return back.reshape(2, chosen.shape[0], page_len, width)

    fetched = collect(spread(kv_pair), mates)
    key_set = jnp.concatenate([k_page[None], fetched[0]], 0).reshape(-1, width)
    value_set = jnp.concatenate([v_page[None], fetched[1]], 0).reshape(-1, width)
    bucket_ids = buckets[0, 0]
    one_hot = bucket_ids[..., None] == jnp.arange(bias_table.shape[0], dtype=jnp.int32)
    bias_blocks = jnp.sum(jnp.where(one_hot[..., None], bias_table, 0.0), axis=-2)
    allowed = jnp.concatenate(
        [jnp.ones((1, block_count, block_count), bool), block_mask[0, 0] == 1], 0
    )
    attn, prob, prob_b = attend_forward(q_page, key_set, value_set, bias_blocks, allowed)
    partial = lax.dot_general(
        attn, g_page, (((0,), (0,)), ((), ())), preferred_element_type=jnp.float32
    )
    dp_size = lax.axis_size("dp")
    rows_each = width // (dp_size * peers)
    partial = partial.reshape(dp_size, peers, rows_each, width)
    partial = halving_scatter(partial, "dp", dp_size)
    partial = lax.all_to_all(partial, "page", split_axis=1, concat_axis=1, tiled=True)
    weight_grad = jnp.sum(partial, axis=(0, 1))
    q_grad, k_grad, v_grad = attend_backward(
        q_page, key_set, value_set, d_attn, attn, prob, prob_b
    )
    layer_out = jnp.dot(attn, weight, preferred_element_type=jnp.float32).astype(jnp.bfloat16)
    outgoing = (
        jnp.stack([k_grad[page_len:], v_grad[page_len:]])
        .reshape(2, ROUNDS, page_len, width)
        .astype(jnp.bfloat16)
    )

    def give_back(terms, chosen):
        round_count = terms.shape[1]
        pieces = terms.reshape(2, round_count, peers, piece_rows, width)
        received = lax.all_to_all(pieces, "page", split_axis=2, concat_axis=2, tiled=True)
        picked = jnp.stack(
            [jnp.take(received[:, r], chosen[r], axis=1) for r in range(round_count)], 1
        )
        back = lax.all_to_all(picked, "page", split_axis=2, concat_axis=2, tiled=True)
        return back.reshape(2, round_count, page_len, width)

    returned = give_back(outgoing, mates)
    totals = jnp.stack([k_grad[:page_len], v_grad[:page_len]]) + jnp.sum(
        returned.astype(jnp.float32), axis=1
    )
    key_grad = totals[0].astype(jnp.bfloat16)[None, None]
    value_grad = totals[1].astype(jnp.bfloat16)[None, None]
    return (
        layer_out[None, None],
        q_grad.astype(jnp.bfloat16)[None, None],
        key_grad,
        value_grad,
        weight_grad,
    )


def solution(mesh):
    in_specs = (
        P("dp", "page", None, None),
        P("dp", "page", None, None),
        P("dp", "page", None, None),
        P("dp", "page", None, None),
        P(("dp", "page"), None),
        P("dp", None, None),
        P("dp", "page", None, None, None),
        P("dp", "page", None, None, None),
        P(),
    )
    out_specs = (
        P("dp", "page", None, None),
        P("dp", "page", None, None),
        P("dp", "page", None, None),
        P("dp", "page", None, None),
        P(("dp", "page"), None),
    )
    return jax.shard_map(shards, mesh=mesh, in_specs=in_specs, out_specs=out_specs, check_vma=False)
```

```python
import math

import jax
import jax.numpy as jnp
from jax import lax
from jax.sharding import PartitionSpec as P

H = 16
BLOCK = 128
ROUNDS = 2


neg_large = -1e30


def attend_forward(query_rows, key_set, value_set, bias_blocks, allowed):
    page_len, width = query_rows.shape
    key_count = key_set.shape[0]
    groups = key_count // page_len
    head_dim = width // H
    block_count = page_len // BLOCK
    scale = 1.0 / math.sqrt(head_dim)
    q = query_rows.reshape(page_len, H, head_dim)
    k = key_set.reshape(key_count, H, head_dim)
    v = value_set.reshape(key_count, H, head_dim)
    scores = jnp.einsum("qhd,khd->hqk", q, k, preferred_element_type=jnp.float32) * scale
    scores = scores.reshape(H, block_count, BLOCK, groups, block_count, BLOCK)
    bias_wide = bias_blocks.transpose(3, 1, 0, 2)[:, :, None, :, :, None]
    scores = scores + bias_wide
    allow_wide = allowed.transpose(1, 0, 2)[None, :, None, :, :, None]
    scores = jnp.where(allow_wide, scores, neg_large).reshape(H, page_len, key_count)
    top = jnp.max(scores, axis=-1, keepdims=True)
    expo = jnp.exp(scores - top)
    prob = expo / jnp.sum(expo, axis=-1, keepdims=True)
    prob_b = prob.astype(jnp.bfloat16)
    attn = jnp.einsum("hqk,khd->qhd", prob_b, v, preferred_element_type=jnp.float32).astype(
        jnp.bfloat16
    )
    return attn.reshape(page_len, width), prob, prob_b


def attend_backward(query_rows, key_set, value_set, grad_rows, attn, prob, prob_b):
    page_len, width = query_rows.shape
    key_count = key_set.shape[0]
    head_dim = width // H
    scale = 1.0 / math.sqrt(head_dim)
    q = query_rows.reshape(page_len, H, head_dim)
    k = key_set.reshape(key_count, H, head_dim)
    v = value_set.reshape(key_count, H, head_dim)
    g = grad_rows.reshape(page_len, H, head_dim)
    a = attn.reshape(page_len, H, head_dim)
    dprob = jnp.einsum("qhd,khd->hqk", g, v, preferred_element_type=jnp.float32)
    row_dot = jnp.sum(g.astype(jnp.float32) * a.astype(jnp.float32), axis=-1).T[:, :, None]
    dscore = (prob * (dprob - row_dot) * scale).astype(jnp.bfloat16)
    q_grad = jnp.einsum("hqk,khd->qhd", dscore, k, preferred_element_type=jnp.float32)
    k_grad = jnp.einsum("hqk,qhd->khd", dscore, q, preferred_element_type=jnp.float32)
    v_grad = jnp.einsum("hqk,qhd->khd", prob_b, g, preferred_element_type=jnp.float32)
    return (
        q_grad.reshape(page_len, width),
        k_grad.reshape(key_count, width),
        v_grad.reshape(key_count, width),
    )


def doubling_gather(block, axis, size):
    if size & (size - 1) or size < 16:
        return lax.all_gather(block, axis, axis=0, tiled=True)
    me = lax.axis_index(axis)
    bits = [size // 2, 2] + [b for b in (size // 4, 1) if b not in (size // 2, 2)]
    bits += [1 << k for k in range(size.bit_length() - 1) if (1 << k) not in bits]
    held = block[None]
    for b in bits:
        upper = (me // b) % 2 == 1
        got = lax.ppermute(held, axis, perm=[(i, i ^ b) for i in range(size)])
        held = jnp.stack([jnp.where(upper, got, held), jnp.where(upper, held, got)])
    count = len(bits)
    held = held.reshape((2,) * count + block.shape)
    axis_bits = bits[::-1]
    order = sorted(range(count), key=lambda i: -axis_bits[i])
    held = held.transpose(order + [count, count + 1])
    return held.reshape(size * block.shape[0], block.shape[1])


def halving_scatter(blocks, axis, size):
    if size & (size - 1):
        return lax.psum_scatter(blocks, axis, scatter_dimension=0, tiled=True)
    me = lax.axis_index(axis)
    half = size // 2
    while half >= 1:
        upper = (me // half) % 2
        keep = lax.dynamic_slice_in_dim(blocks, upper * half, half, axis=0)
        send = lax.dynamic_slice_in_dim(blocks, (1 - upper) * half, half, axis=0)
        pairs = [(i, i ^ half) for i in range(size)]
        blocks = keep + lax.ppermute(send, axis, perm=pairs)
        half //= 2
    return blocks


def shards(queries, keys, values, grad_out, out_weight, partners, block_mask, buckets, bias_table):
    page_count = lax.axis_size("page")
    copies = jnp.broadcast_to(out_weight[None], (page_count,) + out_weight.shape)
    near = lax.all_to_all(copies, "page", split_axis=0, concat_axis=0, tiled=True)
    near = near.reshape(page_count * out_weight.shape[0], out_weight.shape[1])
    weight = doubling_gather(near, "dp", lax.axis_size("dp"))
    q_page = queries[0, 0]
    k_page = keys[0, 0]
    v_page = values[0, 0]
    g_page = grad_out[0, 0]
    page_len, width = q_page.shape
    block_count = page_len // BLOCK
    peers = lax.axis_size("page")
    piece_rows = page_len // peers
    mates = partners[0]
    kv_pair = jnp.stack([k_page, v_page])
    d_attn = lax.dot_general(
        g_page, weight, (((1,), (1,)), ((), ())), preferred_element_type=jnp.float32
    ).astype(jnp.bfloat16)

    def spread(stacked):
        pieces = stacked.reshape(2, peers, piece_rows, width)
        return lax.all_to_all(pieces, "page", split_axis=1, concat_axis=1, tiled=True)

    def collect(received, chosen):
        picked = jnp.take(received, chosen, axis=1)
        back = lax.all_to_all(picked, "page", split_axis=2, concat_axis=2, tiled=True)
        return back.reshape(2, chosen.shape[0], page_len, width)

    fetched = collect(spread(kv_pair), mates)
    key_set = jnp.concatenate([k_page[None], fetched[0]], 0).reshape(-1, width)
    value_set = jnp.concatenate([v_page[None], fetched[1]], 0).reshape(-1, width)
    bucket_ids = buckets[0, 0]
    one_hot = bucket_ids[..., None] == jnp.arange(bias_table.shape[0], dtype=jnp.int32)
    bias_blocks = jnp.sum(jnp.where(one_hot[..., None], bias_table, 0.0), axis=-2)
    allowed = jnp.concatenate(
        [jnp.ones((1, block_count, block_count), bool), block_mask[0, 0] == 1], 0
    )
    attn, prob, prob_b = attend_forward(q_page, key_set, value_set, bias_blocks, allowed)
    partial = lax.dot_general(
        attn, g_page, (((0,), (0,)), ((), ())), preferred_element_type=jnp.float32
    )
    dp_size = lax.axis_size("dp")
    rows_each = width // (dp_size * peers)
    partial = partial.reshape(dp_size, peers, rows_each, width)
    partial = halving_scatter(partial, "dp", dp_size)
    partial = lax.all_to_all(partial, "page", split_axis=1, concat_axis=1, tiled=True)
    weight_grad = jnp.sum(partial, axis=(0, 1))
    q_grad, k_grad, v_grad = attend_backward(
        q_page, key_set, value_set, d_attn, attn, prob, prob_b
    )
    layer_out = jnp.dot(attn, weight, preferred_element_type=jnp.float32).astype(jnp.bfloat16)
    outgoing = (
        jnp.stack([k_grad[page_len:], v_grad[page_len:]])
        .reshape(2, ROUNDS, page_len, width)
        .astype(jnp.bfloat16)
    )

    def give_back(terms, chosen):
        round_count = terms.shape[1]
        pieces = terms.reshape(2, round_count, peers, piece_rows, width)
        received = lax.all_to_all(pieces, "page", split_axis=2, concat_axis=2, tiled=True)
        picked = jnp.stack(
            [jnp.take(received[:, r], chosen[r], axis=1) for r in range(round_count)], 1
        )
        back = lax.all_to_all(picked, "page", split_axis=2, concat_axis=2, tiled=True)
        return back.reshape(2, round_count, page_len, width)

    returned = give_back(outgoing, mates)
    totals = jnp.stack([k_grad[:page_len], v_grad[:page_len]]) + jnp.sum(
        returned.astype(jnp.float32), axis=1
    )
    key_grad = totals[0].astype(jnp.bfloat16)[None, None]
    value_grad = totals[1].astype(jnp.bfloat16)[None, None]
    return (
        layer_out[None, None],
        q_grad.astype(jnp.bfloat16)[None, None],
        key_grad,
        value_grad,
        weight_grad,
    )


def solution(mesh):
    in_specs = (
        P("dp", "page", None, None),
        P("dp", "page", None, None),
        P("dp", "page", None, None),
        P("dp", "page", None, None),
        P(("dp", "page"), None),
        P("dp", None, None),
        P("dp", "page", None, None, None),
        P("dp", "page", None, None, None),
        P(),
    )
    out_specs = (
        P("dp", "page", None, None),
        P("dp", "page", None, None),
        P("dp", "page", None, None),
        P("dp", "page", None, None),
        P(("dp", "page"), None),
    )
    return jax.shard_map(shards, mesh=mesh, in_specs=in_specs, out_specs=out_specs, check_vma=False)
```

```python
import math

import jax
import jax.numpy as jnp
from jax import lax
from jax.sharding import PartitionSpec as P

H = 16
BLOCK = 128
ROUNDS = 2


neg_large = -1e30


def attend_forward(query_rows, key_set, value_set, bias_blocks, allowed):
    page_len, width = query_rows.shape
    key_count = key_set.shape[0]
    groups = key_count // page_len
    head_dim = width // H
    block_count = page_len // BLOCK
    scale = 1.0 / math.sqrt(head_dim)
    q = query_rows.reshape(page_len, H, head_dim)
    k = key_set.reshape(key_count, H, head_dim)
    v = value_set.reshape(key_count, H, head_dim)
    scores = jnp.einsum("qhd,khd->hqk", q, k, preferred_element_type=jnp.float32) * scale
    scores = scores.reshape(H, block_count, BLOCK, groups, block_count, BLOCK)
    bias_wide = bias_blocks.transpose(3, 1, 0, 2)[:, :, None, :, :, None]
    scores = scores + bias_wide
    allow_wide = allowed.transpose(1, 0, 2)[None, :, None, :, :, None]
    scores = jnp.where(allow_wide, scores, neg_large).reshape(H, page_len, key_count)
    top = jnp.max(scores, axis=-1, keepdims=True)
    expo = jnp.exp(scores - top)
    prob = expo / jnp.sum(expo, axis=-1, keepdims=True)
    prob_b = prob.astype(jnp.bfloat16)
    attn = jnp.einsum("hqk,khd->qhd", prob_b, v, preferred_element_type=jnp.float32).astype(
        jnp.bfloat16
    )
    return attn.reshape(page_len, width), prob, prob_b


def attend_backward(query_rows, key_set, value_set, grad_rows, attn, prob, prob_b):
    page_len, width = query_rows.shape
    key_count = key_set.shape[0]
    head_dim = width // H
    scale = 1.0 / math.sqrt(head_dim)
    q = query_rows.reshape(page_len, H, head_dim)
    k = key_set.reshape(key_count, H, head_dim)
    v = value_set.reshape(key_count, H, head_dim)
    g = grad_rows.reshape(page_len, H, head_dim)
    a = attn.reshape(page_len, H, head_dim)
    dprob = jnp.einsum("qhd,khd->hqk", g, v, preferred_element_type=jnp.float32)
    row_dot = jnp.sum(g.astype(jnp.float32) * a.astype(jnp.float32), axis=-1).T[:, :, None]
    dscore = (prob * (dprob - row_dot) * scale).astype(jnp.bfloat16)
    q_grad = jnp.einsum("hqk,khd->qhd", dscore, k, preferred_element_type=jnp.float32)
    k_grad = jnp.einsum("hqk,qhd->khd", dscore, q, preferred_element_type=jnp.float32)
    v_grad = jnp.einsum("hqk,qhd->khd", prob_b, g, preferred_element_type=jnp.float32)
    return (
        q_grad.reshape(page_len, width),
        k_grad.reshape(key_count, width),
        v_grad.reshape(key_count, width),
    )


def halving_scatter(blocks, axis, size):
    if size & (size - 1) or size < 16:
        return lax.psum_scatter(blocks, axis, scatter_dimension=0, tiled=True)
    me = lax.axis_index(axis)
    count = size.bit_length() - 1
    axis_bits = [size >> (k + 1) for k in range(count)]
    order = [1, size // 4, size // 2, 2] + [b for b in axis_bits if b not in (1, 2, size // 4, size // 2)]
    rest = blocks.shape[1:]
    blocks = blocks.reshape((2,) * count + rest)
    for b in order:
        at = axis_bits.index(b)
        upper = (me // b) % 2
        keep = lax.dynamic_index_in_dim(blocks, upper, axis=at, keepdims=False)
        send = lax.dynamic_index_in_dim(blocks, 1 - upper, axis=at, keepdims=False)
        pairs = [(i, i ^ b) for i in range(size)]
        blocks = keep + lax.ppermute(send, axis, perm=pairs)
        axis_bits.pop(at)
    return blocks.reshape((1,) + rest)


def shards(queries, keys, values, grad_out, out_weight, partners, block_mask, buckets, bias_table):
    page_count = lax.axis_size("page")
    copies = jnp.broadcast_to(out_weight[None], (page_count,) + out_weight.shape)
    near = lax.all_to_all(copies, "page", split_axis=0, concat_axis=0, tiled=True)
    near = near.reshape(page_count * out_weight.shape[0], out_weight.shape[1])
    weight = lax.all_gather(near, "dp", axis=0, tiled=True)
    q_page = queries[0, 0]
    k_page = keys[0, 0]
    v_page = values[0, 0]
    g_page = grad_out[0, 0]
    page_len, width = q_page.shape
    block_count = page_len // BLOCK
    peers = lax.axis_size("page")
    piece_rows = page_len // peers
    mates = partners[0]
    kv_pair = jnp.stack([k_page, v_page])
    d_attn = lax.dot_general(
        g_page, weight, (((1,), (1,)), ((), ())), preferred_element_type=jnp.float32
    ).astype(jnp.bfloat16)

    def spread(stacked):
        pieces = stacked.reshape(2, peers, piece_rows, width)
        return lax.all_to_all(pieces, "page", split_axis=1, concat_axis=1, tiled=True)

    def collect(received, chosen):
        picked = jnp.take(received, chosen, axis=1)
        back = lax.all_to_all(picked, "page", split_axis=2, concat_axis=2, tiled=True)
        return back.reshape(2, chosen.shape[0], page_len, width)

    fetched = collect(spread(kv_pair), mates)
    key_set = jnp.concatenate([k_page[None], fetched[0]], 0).reshape(-1, width)
    value_set = jnp.concatenate([v_page[None], fetched[1]], 0).reshape(-1, width)
    bucket_ids = buckets[0, 0]
    one_hot = bucket_ids[..., None] == jnp.arange(bias_table.shape[0], dtype=jnp.int32)
    bias_blocks = jnp.sum(jnp.where(one_hot[..., None], bias_table, 0.0), axis=-2)
    allowed = jnp.concatenate(
        [jnp.ones((1, block_count, block_count), bool), block_mask[0, 0] == 1], 0
    )
    attn, prob, prob_b = attend_forward(q_page, key_set, value_set, bias_blocks, allowed)
    partial = lax.dot_general(
        attn, g_page, (((0,), (0,)), ((), ())), preferred_element_type=jnp.float32
    )
    dp_size = lax.axis_size("dp")
    rows_each = width // (dp_size * peers)
    partial = partial.reshape(dp_size, peers, rows_each, width)
    partial = halving_scatter(partial, "dp", dp_size)
    partial = lax.all_to_all(partial, "page", split_axis=1, concat_axis=1, tiled=True)
    weight_grad = jnp.sum(partial, axis=(0, 1))
    q_grad, k_grad, v_grad = attend_backward(
        q_page, key_set, value_set, d_attn, attn, prob, prob_b
    )
    layer_out = jnp.dot(attn, weight, preferred_element_type=jnp.float32).astype(jnp.bfloat16)
    outgoing = (
        jnp.stack([k_grad[page_len:], v_grad[page_len:]])
        .reshape(2, ROUNDS, page_len, width)
        .astype(jnp.bfloat16)
    )

    def give_back(terms, chosen):
        round_count = terms.shape[1]
        pieces = terms.reshape(2, round_count, peers, piece_rows, width)
        received = lax.all_to_all(pieces, "page", split_axis=2, concat_axis=2, tiled=True)
        picked = jnp.stack(
            [jnp.take(received[:, r], chosen[r], axis=1) for r in range(round_count)], 1
        )
        back = lax.all_to_all(picked, "page", split_axis=2, concat_axis=2, tiled=True)
        return back.reshape(2, round_count, page_len, width)

    returned = give_back(outgoing, mates)
    totals = jnp.stack([k_grad[:page_len], v_grad[:page_len]]) + jnp.sum(
        returned.astype(jnp.float32), axis=1
    )
    key_grad = totals[0].astype(jnp.bfloat16)[None, None]
    value_grad = totals[1].astype(jnp.bfloat16)[None, None]
    return (
        layer_out[None, None],
        q_grad.astype(jnp.bfloat16)[None, None],
        key_grad,
        value_grad,
        weight_grad,
    )


def solution(mesh):
    in_specs = (
        P("dp", "page", None, None),
        P("dp", "page", None, None),
        P("dp", "page", None, None),
        P("dp", "page", None, None),
        P(("dp", "page"), None),
        P("dp", None, None),
        P("dp", "page", None, None, None),
        P("dp", "page", None, None, None),
        P(),
    )
    out_specs = (
        P("dp", "page", None, None),
        P("dp", "page", None, None),
        P("dp", "page", None, None),
        P("dp", "page", None, None),
        P(("dp", "page"), None),
    )
    return jax.shard_map(shards, mesh=mesh, in_specs=in_specs, out_specs=out_specs, check_vma=False)
```

```python
import math

import jax
import jax.numpy as jnp
from jax import lax
from jax.sharding import PartitionSpec as P

H = 16
BLOCK = 128
ROUNDS = 2


neg_large = -1e30


def attend_forward(query_rows, key_set, value_set, bias_blocks, allowed):
    page_len, width = query_rows.shape
    key_count = key_set.shape[0]
    groups = key_count // page_len
    head_dim = width // H
    block_count = page_len // BLOCK
    scale = 1.0 / math.sqrt(head_dim)
    q = query_rows.reshape(page_len, H, head_dim)
    k = key_set.reshape(key_count, H, head_dim)
    v = value_set.reshape(key_count, H, head_dim)
    scores = jnp.einsum("qhd,khd->hqk", q, k, preferred_element_type=jnp.float32) * scale
    scores = scores.reshape(H, block_count, BLOCK, groups, block_count, BLOCK)
    bias_wide = bias_blocks.transpose(3, 1, 0, 2)[:, :, None, :, :, None]
    scores = scores + bias_wide
    allow_wide = allowed.transpose(1, 0, 2)[None, :, None, :, :, None]
    scores = jnp.where(allow_wide, scores, neg_large).reshape(H, page_len, key_count)
    top = jnp.max(scores, axis=-1, keepdims=True)
    expo = jnp.exp(scores - top)
    prob = expo / jnp.sum(expo, axis=-1, keepdims=True)
    prob_b = prob.astype(jnp.bfloat16)
    attn = jnp.einsum("hqk,khd->qhd", prob_b, v, preferred_element_type=jnp.float32).astype(
        jnp.bfloat16
    )
    return attn.reshape(page_len, width), prob, prob_b


def attend_backward(query_rows, key_set, value_set, grad_rows, attn, prob, prob_b):
    page_len, width = query_rows.shape
    key_count = key_set.shape[0]
    head_dim = width // H
    scale = 1.0 / math.sqrt(head_dim)
    q = query_rows.reshape(page_len, H, head_dim)
    k = key_set.reshape(key_count, H, head_dim)
    v = value_set.reshape(key_count, H, head_dim)
    g = grad_rows.reshape(page_len, H, head_dim)
    a = attn.reshape(page_len, H, head_dim)
    dprob = jnp.einsum("qhd,khd->hqk", g, v, preferred_element_type=jnp.float32)
    row_dot = jnp.sum(g.astype(jnp.float32) * a.astype(jnp.float32), axis=-1).T[:, :, None]
    dscore = (prob * (dprob - row_dot) * scale).astype(jnp.bfloat16)
    q_grad = jnp.einsum("hqk,khd->qhd", dscore, k, preferred_element_type=jnp.float32)
    k_grad = jnp.einsum("hqk,qhd->khd", dscore, q, preferred_element_type=jnp.float32)
    v_grad = jnp.einsum("hqk,qhd->khd", prob_b, g, preferred_element_type=jnp.float32)
    return (
        q_grad.reshape(page_len, width),
        k_grad.reshape(key_count, width),
        v_grad.reshape(key_count, width),
    )


def halving_scatter(blocks, axis, size):
    if size & (size - 1):
        return lax.psum_scatter(blocks, axis, scatter_dimension=0, tiled=True)
    me = lax.axis_index(axis)
    half = size // 2
    while half >= 1:
        upper = (me // half) % 2
        keep = lax.dynamic_slice_in_dim(blocks, upper * half, half, axis=0)
        send = lax.dynamic_slice_in_dim(blocks, (1 - upper) * half, half, axis=0)
        pairs = [(i, i ^ half) for i in range(size)]
        blocks = keep + lax.ppermute(send, axis, perm=pairs)
        half //= 2
    return blocks


def shards(queries, keys, values, grad_out, out_weight, partners, block_mask, buckets, bias_table):
    q_page = queries[0, 0]
    k_page = keys[0, 0]
    v_page = values[0, 0]
    g_page = grad_out[0, 0]
    page_len, width = q_page.shape
    block_count = page_len // BLOCK
    peers = lax.axis_size("page")
    piece_rows = page_len // peers
    mates = partners[0]
    kv_pair = jnp.stack([k_page, v_page])

    def spread(stacked):
        pieces = stacked.reshape(2, peers, piece_rows, width)
        return lax.all_to_all(pieces, "page", split_axis=1, concat_axis=1, tiled=True)

    def collect(received, chosen):
        picked = jnp.take(received, chosen, axis=1)
        back = lax.all_to_all(picked, "page", split_axis=2, concat_axis=2, tiled=True)
        return back.reshape(2, chosen.shape[0], page_len, width)

    shard_rows = out_weight.shape[0]
    copies = jnp.broadcast_to(out_weight[None], (peers,) + out_weight.shape)
    kv_pieces = kv_pair.reshape(2, peers, piece_rows, width).transpose(1, 0, 2, 3)
    joint = jnp.concatenate([kv_pieces.reshape(peers, 2 * piece_rows, width), copies], 1)
    joint = lax.all_to_all(joint, "page", split_axis=0, concat_axis=0, tiled=True)
    near = joint[:, 2 * piece_rows :].reshape(peers * shard_rows, width)
    weight = lax.all_gather(near, "dp", axis=0, tiled=True)
    received = joint[:, : 2 * piece_rows].reshape(peers, 2, piece_rows, width)
    fetched = collect(received.transpose(1, 0, 2, 3), mates)
    d_attn = lax.dot_general(
        g_page, weight, (((1,), (1,)), ((), ())), preferred_element_type=jnp.float32
    ).astype(jnp.bfloat16)
    key_set = jnp.concatenate([k_page[None], fetched[0]], 0).reshape(-1, width)
    value_set = jnp.concatenate([v_page[None], fetched[1]], 0).reshape(-1, width)
    bucket_ids = buckets[0, 0]
    one_hot = bucket_ids[..., None] == jnp.arange(bias_table.shape[0], dtype=jnp.int32)
    bias_blocks = jnp.sum(jnp.where(one_hot[..., None], bias_table, 0.0), axis=-2)
    allowed = jnp.concatenate(
        [jnp.ones((1, block_count, block_count), bool), block_mask[0, 0] == 1], 0
    )
    attn, prob, prob_b = attend_forward(q_page, key_set, value_set, bias_blocks, allowed)
    partial = lax.dot_general(
        attn, g_page, (((0,), (0,)), ((), ())), preferred_element_type=jnp.float32
    )
    dp_size = lax.axis_size("dp")
    rows_each = width // (dp_size * peers)
    partial = partial.reshape(dp_size, peers, rows_each, width)
    partial = halving_scatter(partial, "dp", dp_size)
    partial = lax.all_to_all(partial, "page", split_axis=1, concat_axis=1, tiled=True)
    weight_grad = jnp.sum(partial, axis=(0, 1))
    q_grad, k_grad, v_grad = attend_backward(
        q_page, key_set, value_set, d_attn, attn, prob, prob_b
    )
    layer_out = jnp.dot(attn, weight, preferred_element_type=jnp.float32).astype(jnp.bfloat16)
    outgoing = (
        jnp.stack([k_grad[page_len:], v_grad[page_len:]])
        .reshape(2, ROUNDS, page_len, width)
        .astype(jnp.bfloat16)
    )

    def give_back(terms, chosen):
        round_count = terms.shape[1]
        pieces = terms.reshape(2, round_count, peers, piece_rows, width)
        received = lax.all_to_all(pieces, "page", split_axis=2, concat_axis=2, tiled=True)
        picked = jnp.stack(
            [jnp.take(received[:, r], chosen[r], axis=1) for r in range(round_count)], 1
        )
        back = lax.all_to_all(picked, "page", split_axis=2, concat_axis=2, tiled=True)
        return back.reshape(2, round_count, page_len, width)

    returned = give_back(outgoing, mates)
    totals = jnp.stack([k_grad[:page_len], v_grad[:page_len]]) + jnp.sum(
        returned.astype(jnp.float32), axis=1
    )
    key_grad = totals[0].astype(jnp.bfloat16)[None, None]
    value_grad = totals[1].astype(jnp.bfloat16)[None, None]
    return (
        layer_out[None, None],
        q_grad.astype(jnp.bfloat16)[None, None],
        key_grad,
        value_grad,
        weight_grad,
    )


def solution(mesh):
    in_specs = (
        P("dp", "page", None, None),
        P("dp", "page", None, None),
        P("dp", "page", None, None),
        P("dp", "page", None, None),
        P(("dp", "page"), None),
        P("dp", None, None),
        P("dp", "page", None, None, None),
        P("dp", "page", None, None, None),
        P(),
    )
    out_specs = (
        P("dp", "page", None, None),
        P("dp", "page", None, None),
        P("dp", "page", None, None),
        P("dp", "page", None, None),
        P(("dp", "page"), None),
    )
    return jax.shard_map(shards, mesh=mesh, in_specs=in_specs, out_specs=out_specs, check_vma=False)
```
